512 devices in a mesh: ctx: 64 (over y, z), kvh: 8 (over x, core).
Axes of the slice: x: 4, y: 4, z: 16, core: 2. Of those that a mesh axis runs over, the one named last changes fastest.
Arguments:
- queries: bfloat16 [16384, 8192], P('ctx', 'kvh'), may hold values from -256 to 256
- keys: bfloat16 [16384, 1024], P('ctx', 'kvh'), may hold values from -4 to 4
- values: bfloat16 [16384, 1024], P('ctx', 'kvh'), may hold values from -6 to 6
- selection: int32 [8, 256, 16], P('kvh', 'ctx'), may hold values from -1 to 250, as said below
Outputs:
- attention_out: bfloat16 [16384, 8192], P(('ctx', 'kvh'))
The draws below stay inside these ranges and needn't reach their ends.
Inputs may be any that keep to these rules, and one draw needn't show every extreme that they name: `selection`: entries -1 stand after the named tiles; the tiles of one list are distinct and each is at most b - 256 / 64 - 1 for block b. The query blocks held by one index of ctx (blocks c * 4 to (c + 1) * 4 - 1) name, together, at most 2 distinct tiles of any one other such group of blocks, and only tiles of earlier groups; some group reaches 2 in every draw.
All inputs are finite; a program needn't handle non-finite values.
Results may differ from the reference program's by a relative error of at most 0.008.
Values may be sent and summed in bfloat16 or wider, within the bound.
No kernel may reach another device: no remote copies, remote signals or barrier semaphores. Data moves between devices by JAX's collectives and lax.ppermute only.
A program may use at most 64 MiB of HBM per device.

```python
import jax
import jax.numpy as jnp
from jax import lax

HQ = 8
DH = 128
TILE = 64
SEL = 16
WINDOW = 256
MOST = 2
TOK_DEV = 256
KVH = 8
SEQ = 16384


def draw_pair(key):
    keys_base = jax.random.truncated_normal(jax.random.fold_in(key, 11), -4.0, 4.0, (SEQ, KVH, DH), jnp.float32)
    query_base = jax.random.truncated_normal(jax.random.fold_in(key, 12), -4.0, 4.0, (SEQ, KVH, HQ, DH), jnp.float32)
    keys_out = keys_base
    query_out = query_base
    return (query_out.reshape(SEQ, KVH * HQ * DH), keys_out.reshape(SEQ, KVH * DH))


def draw_queries(key, part):
    return draw_pair(key)[0].astype(jnp.bfloat16)


def draw_keys(key, part):
    return draw_pair(key)[1].astype(jnp.bfloat16)


def draw_selection(key, part):
    blocks = SEQ // TILE
    per_dev = TOK_DEV // TILE
    devices = SEQ // TOK_DEV
    reach_tiles = WINDOW // TILE
    tile_ids = jnp.arange(blocks, dtype=jnp.int32)
    owners = tile_ids // per_dev
    slot_identifiers = jnp.arange(per_dev, dtype=jnp.int32)
    holder_identifiers = jnp.arange(devices, dtype=jnp.int32)

    def one_head(head_key):
        slot_ranking_value = jax.random.randint(jax.random.fold_in(head_key, 1), (devices, devices, per_dev), 0, 1 << 12) * per_dev + slot_identifiers[None, None, :]
        anchor_token_boost = jnp.where((holder_identifiers[:, None] == 0) & (slot_identifiers[None, :] == 0), 1 << 20, 0)
        slot_ranking_value = slot_ranking_value + anchor_token_boost[None, :, :]
        order = jnp.argsort(-slot_ranking_value, axis=-1, stable=True)
        ranks = jnp.argsort(order, axis=-1, stable=True)
        pooled = ranks < MOST
        slot_of = pooled[:, owners, tile_ids % per_dev]
        in_pool = (owners[None, :] < holder_identifiers[:, None]) & slot_of
        block_pool = in_pool[tile_ids // per_dev]
        eligible = block_pool & (tile_ids[None, :] <= tile_ids[:, None] - reach_tiles - 1)
        nearness = owners[None, :] * ((1 << 16) // devices)
        noise_draw = (jax.random.randint(jax.random.fold_in(head_key, 2), (blocks, blocks), 0, 1 << 16) + nearness) * blocks + tile_ids[None, :]
        reader_device = (tile_ids // per_dev)[:, None]
        far_owner = (reader_device >= devices // 2) & (owners[None, :] == reader_device - devices // 2)
        noise_draw = noise_draw + jnp.where(far_owner, 1 << 28, 0)
        ranked = jnp.where(eligible, noise_draw, -1)
        top_values, top_index = lax.top_k(ranked, SEL)
        return jnp.where(top_values >= 0, top_index, -1).astype(jnp.int32)
    per_head_keys = jax.random.split(jax.random.fold_in(key, 21), KVH)
    return jax.vmap(one_head)(per_head_keys)


def block_levels(own_key, shape, pieces, smallest, largest):
    factor_of, own = 1.0, jax.random.fold_in(own_key, 6)
    for dim, parts in pieces:
        draws = jnp.exp(jax.random.uniform(jax.random.fold_in(own, dim), (parts,), jnp.float32, smallest / len(pieces), largest / len(pieces)))
        factor_of = factor_of * jnp.repeat(draws, shape[dim] // parts).reshape([-1 if axis == dim else 1 for axis in range(len(shape))])
    return factor_of


def gaussian(rng, dims, deviation, reach, shards=(), kind=jnp.bfloat16):
    values = jax.random.normal(rng, dims, jnp.float32) * deviation
    if len(shards) > 0:
        values = block_levels(rng, dims, shards, -0.22, 0.18) * values
    return jnp.clip(values, min=-reach, max=reach).astype(kind)


def setup_inputs(seed: int = 0) -> dict:
    seeds = jax.random.split(jax.random.key(seed), 5)
    return {
        "queries": draw_queries(jax.random.fold_in(seeds[4], 71), 0),
        "keys": draw_keys(jax.random.fold_in(seeds[4], 71), 0),
        "values": gaussian(seeds[2], (SEQ, KVH * DH), 1.0, 6.0, ((0, 64), (1, 8))),
        "selection": draw_selection(jax.random.fold_in(seeds[4], 71), 0),
    }


masked_score = -1.0e30


def block_attention_step(query_rows, window_keys, window_values, window_ok, chosen_keys, chosen_values, chosen_ok, scale):
    query_f = query_rows.astype(jnp.float32)
    win_scores = jnp.einsum("rhd,jd->hrj", query_f, window_keys.astype(jnp.float32), precision=lax.Precision.HIGHEST) * scale
    sel_scores = jnp.einsum("rhd,jd->hrj", query_f, chosen_keys.astype(jnp.float32), precision=lax.Precision.HIGHEST) * scale
    win_scores = jnp.where(window_ok[None, :, :], win_scores, masked_score)
    sel_scores = jnp.where(chosen_ok[None, None, :], sel_scores, masked_score)
    peak = jnp.maximum(jnp.max(win_scores, axis=-1), jnp.max(sel_scores, axis=-1))
    win_weights = jnp.exp(win_scores - peak[:, :, None])
    sel_weights = jnp.exp(sel_scores - peak[:, :, None])
    total = jnp.sum(win_weights, axis=-1) + jnp.sum(sel_weights, axis=-1)
    numerator = jnp.einsum("hrj,jd->rhd", win_weights.astype(jnp.bfloat16).astype(jnp.float32), window_values.astype(jnp.float32), precision=lax.Precision.HIGHEST)
    numerator = numerator + jnp.einsum("hrj,jd->rhd", sel_weights.astype(jnp.bfloat16).astype(jnp.float32), chosen_values.astype(jnp.float32), precision=lax.Precision.HIGHEST)
    result = numerator / jnp.transpose(total)[:, :, None]
    return result.astype(jnp.bfloat16).reshape(query_rows.shape[0], -1)


def reference(queries, keys, values, selection):
    blocks = SEQ // TILE
    scale = 1.0 / (DH ** 0.5)
    query_heads = jnp.moveaxis(queries.reshape(SEQ, KVH, HQ, DH), 1, 0)
    key_heads = jnp.moveaxis(keys.reshape(SEQ, KVH, DH), 1, 0)
    value_heads = jnp.moveaxis(values.reshape(SEQ, KVH, DH), 1, 0)

    def one_head(args):
        head_queries, per_head_keys, head_values, head_lists = args
        padding = jnp.zeros((WINDOW, DH), per_head_keys.dtype)
        padded_keys = jnp.concatenate([padding, per_head_keys], axis=0)
        padded_values = jnp.concatenate([padding, head_values], axis=0)
        key_tiles = per_head_keys.reshape(blocks, TILE * DH)
        value_tiles = head_values.reshape(blocks, TILE * DH)

        def one_block(inner):
            block_index, block_queries, block_list = inner
            start = (block_index * TILE).astype(jnp.int32)
            window_keys = lax.dynamic_slice_in_dim(padded_keys, start, WINDOW + TILE, 0)
            window_values = lax.dynamic_slice_in_dim(padded_values, start, WINDOW + TILE, 0)
            query_pos = start + jnp.arange(TILE, dtype=jnp.int32)
            key_pos = start - WINDOW + jnp.arange(WINDOW + TILE, dtype=jnp.int32)
            window_ok = (key_pos[None, :] <= query_pos[:, None]) & (key_pos[None, :] > query_pos[:, None] - WINDOW) & (key_pos[None, :] >= 0)
            safe_list = jnp.maximum(block_list, 0).astype(jnp.int32)
            chosen_keys = key_tiles[safe_list].reshape(SEL * TILE, DH)
            chosen_values = value_tiles[safe_list].reshape(SEL * TILE, DH)
            chosen_ok = jnp.repeat(block_list >= 0, TILE)
            return block_attention_step(block_queries, window_keys, window_values, window_ok, chosen_keys, chosen_values, chosen_ok, scale)

        return lax.map(one_block, (jnp.arange(blocks, dtype=jnp.int32), head_queries.reshape(blocks, TILE, HQ, DH), head_lists))

    result = lax.map(one_head, (query_heads, key_heads, value_heads, selection))
    return jnp.moveaxis(result, 0, 2).reshape(SEQ, KVH * HQ * DH)
```

```python
import jax
import jax.numpy as jnp
from jax import lax
from jax.sharding import Mesh
from jax.sharding import PartitionSpec as P

TILE = 64
SEL = 16
WINDOW = 256

masked_score = -1e30


def per_device(queries, keys, values, selection):
    tok_rows, head_size = keys.shape
    per_dev = tok_rows // TILE
    n_y = lax.axis_size("cy")
    n_z = lax.axis_size("cz")
    here = lax.axis_index("cy") * n_z + lax.axis_index("cz")
    scale = 1.0 / head_size**0.5
    heads = queries.shape[1] // head_size

    both = jnp.concatenate([keys, values], axis=0)
    gathered = lax.all_gather(both, "cy", axis=0, tiled=False)
    gathered = lax.all_gather(gathered, "cz", axis=0, tiled=False)
    tiles = gathered.reshape(n_z * n_y * 2 * per_dev, TILE, head_size)

    def tile_row(tile_id, kv):
        owner = tile_id // per_dev
        return (((owner % n_z) * n_y + owner // n_z) * 2 + kv) * per_dev + tile_id % per_dev

    flat_list = selection[0].reshape(-1)
    listed = flat_list >= 0
    safe_list = jnp.maximum(flat_list, 0)
    chosen_keys = jnp.take(tiles, tile_row(safe_list, 0), axis=0).reshape(per_dev, SEL * TILE, head_size)
    chosen_values = jnp.take(tiles, tile_row(safe_list, 1), axis=0).reshape(per_dev, SEL * TILE, head_size)

    prev = jnp.maximum(here - 1, 0)
    prev_rows = lax.dynamic_slice_in_dim(
        tiles, tile_row(prev * per_dev, 0), per_dev, axis=0
    ).reshape(tok_rows, head_size)
    prev_vals = lax.dynamic_slice_in_dim(
        tiles, tile_row(prev * per_dev, 1), per_dev, axis=0
    ).reshape(tok_rows, head_size)
    win_keys_all = jnp.concatenate([prev_rows, keys], axis=0)
    win_vals_all = jnp.concatenate([prev_vals, values], axis=0)
    span = WINDOW + TILE
    win_keys = jnp.stack(
        [win_keys_all[tok_rows - WINDOW + b * TILE : tok_rows - WINDOW + b * TILE + span] for b in range(per_dev)]
    )
    win_vals = jnp.stack(
        [win_vals_all[tok_rows - WINDOW + b * TILE : tok_rows - WINDOW + b * TILE + span] for b in range(per_dev)]
    )

    all_keys = jnp.concatenate([win_keys, chosen_keys], axis=1)
    all_vals = jnp.concatenate([win_vals, chosen_values], axis=1)

    block_index = jnp.arange(per_dev, dtype=jnp.int32)
    query_pos = here * tok_rows + block_index[:, None] * TILE + jnp.arange(TILE, dtype=jnp.int32)[None, :]
    key_pos = here * tok_rows + block_index[:, None] * TILE - WINDOW + jnp.arange(span, dtype=jnp.int32)[None, :]
    window_ok = (
        (key_pos[:, None, :] <= query_pos[:, :, None])
        & (key_pos[:, None, :] > query_pos[:, :, None] - WINDOW)
        & (key_pos[:, None, :] >= 0)
    )
    chosen_ok = jnp.repeat(listed.reshape(per_dev, SEL), TILE, axis=1)
    ok = jnp.concatenate(
        [window_ok, jnp.broadcast_to(chosen_ok[:, None, :], (per_dev, TILE, SEL * TILE))], axis=2
    )

    block_queries = queries.reshape(per_dev, TILE, heads, head_size)
    scores = (
        jnp.einsum("brhd,bjd->bhrj", block_queries, all_keys, preferred_element_type=jnp.float32) * scale
    )
    scores = jnp.where(ok[:, None, :, :], scores, masked_score)
    peak = jnp.max(scores, axis=-1, keepdims=True)
    weights = jnp.exp(scores - peak)
    total = jnp.sum(weights, axis=-1)
    numerator = jnp.einsum(
        "bhrj,bjd->brhd", weights.astype(jnp.bfloat16), all_vals, preferred_element_type=jnp.float32
    )
    result = numerator / jnp.transpose(total, (0, 2, 1))[:, :, :, None]
    attended = result.astype(jnp.bfloat16).reshape(tok_rows, heads * head_size)
    return lax.all_to_all(attended, "kvh", split_axis=0, concat_axis=1, tiled=True)


def solution(mesh):
    devices = mesh.devices
    ctx = devices.shape[0]
    z = len({tuple(d.coords)[2] for d in devices[:, 0]})
    z = z if ctx % z == 0 else ctx
    grid = Mesh(devices.reshape(ctx // z, z, devices.shape[1]), ("cy", "cz", "kvh"))
    row = P(("cy", "cz"), "kvh")
    return jax.shard_map(
        per_device,
        mesh=grid,
        in_specs=(row, row, row, P("kvh", ("cy", "cz"), None)),
        out_specs=P(("cy", "cz", "kvh"), None),
        check_vma=False,
    )
```

```python
import functools

import jax
import jax.numpy as jnp
from jax import lax
from jax.experimental import pallas as pl
from jax.experimental.pallas import tpu as pltpu
from jax.sharding import Mesh
from jax.sharding import PartitionSpec as P

TILE = 64
SEL = 16
WINDOW = 256
WIN_TILES = WINDOW // TILE + 1
SLOTS = WIN_TILES + SEL + 1

masked_score = -1e30


def attention_kernel(rows_ref, q_ref, colmask_ref, tiles_hbm, out_ref, kbuf, vbuf, sems, *, per_dev, scale):
    b = pl.program_id(0)
    head_size = kbuf.shape[1]
    copies = []
    for i in range(SLOTS):
        row = rows_ref[b * SLOTS + i]
        dst = pl.ds(i * TILE, TILE)
        ck = pltpu.make_async_copy(tiles_hbm.at[row], kbuf.at[dst], sems.at[0, i])
        cv = pltpu.make_async_copy(tiles_hbm.at[row + per_dev], vbuf.at[dst], sems.at[1, i])
        ck.start()
        cv.start()
        copies += [ck, cv]
    for c in copies:
        c.wait()
    q = q_ref[...]
    heads = q.shape[1] // head_size
    qs = jnp.concatenate([q[:, h * head_size : (h + 1) * head_size] for h in range(heads)], axis=0)
    s = lax.dot_general(qs, kbuf[...], (((1,), (1,)), ((), ())), preferred_element_type=jnp.float32) * scale
    r = lax.broadcasted_iota(jnp.int32, s.shape, 0) % TILE
    j = lax.broadcasted_iota(jnp.int32, s.shape, 1)
    in_window = (j > r) & (j <= r + WINDOW)
    ok = (colmask_ref[0] > 0) & ((j >= WIN_TILES * TILE) | in_window)
    s = jnp.where(ok, s, masked_score)
    peak = jnp.max(s, axis=1, keepdims=True)
    w = jnp.exp(s - peak)
    total = jnp.sum(w, axis=1, keepdims=True)
    num = jnp.dot(w.astype(jnp.bfloat16), vbuf[...], preferred_element_type=jnp.float32)
    res = (num / total).astype(out_ref.dtype)
    for h in range(heads):
        out_ref[:, h * head_size : (h + 1) * head_size] = res[h * TILE : (h + 1) * TILE]


def block_attention(rows, queries, colmask, tiles, per_dev, scale):
    tok_rows, width = queries.shape
    head_size = tiles.shape[2]
    keys_per_block = SLOTS * TILE
    flops = 4 * tok_rows * width * keys_per_block
    return pl.pallas_call(
        functools.partial(attention_kernel, per_dev=per_dev, scale=scale),
        out_shape=jax.ShapeDtypeStruct((tok_rows, width), queries.dtype),
        grid_spec=pltpu.PrefetchScalarGridSpec(
            num_scalar_prefetch=1,
            grid=(per_dev,),
            in_specs=[
                pl.BlockSpec((TILE, width), lambda b, rows: (b, 0)),
                pl.BlockSpec((1, 1, keys_per_block), lambda b, rows: (b, 0, 0)),
                pl.BlockSpec(memory_space=pl.ANY),
            ],
            out_specs=pl.BlockSpec((TILE, width), lambda b, rows: (b, 0)),
            scratch_shapes=[
                pltpu.VMEM((keys_per_block, head_size), tiles.dtype),
                pltpu.VMEM((keys_per_block, head_size), tiles.dtype),
                pltpu.SemaphoreType.DMA((2, SLOTS)),
            ],
        ),
        cost_estimate=pl.CostEstimate(
            flops=flops,
            transcendentals=tok_rows * (width // head_size) * keys_per_block,
            bytes_accessed=2 * tok_rows * width * 2 + 2 * per_dev * SLOTS * TILE * head_size * 2,
        ),
    )(rows, queries, colmask, tiles)


def per_device(queries, keys, values, selection):
    tok_rows, head_size = keys.shape
    per_dev = tok_rows // TILE
    n_y = lax.axis_size("cy")
    n_z = lax.axis_size("cz")
    here = lax.axis_index("cy") * n_z + lax.axis_index("cz")
    scale = 1.0 / head_size**0.5

    both = jnp.concatenate([keys, values], axis=0)
    gathered = lax.all_gather(both, "cy", axis=0, tiled=False)
    gathered = lax.all_gather(gathered, "cz", axis=0, tiled=False)
    tiles = gathered.reshape(n_z * n_y * 2 * per_dev, TILE, head_size)

    def tile_row(tile_id):
        owner = tile_id // per_dev
        return (((owner % n_z) * n_y + owner // n_z) * 2) * per_dev + tile_id % per_dev

    lists = selection[0]
    listed = lists >= 0
    safe_list = jnp.maximum(lists, 0)
    block_index = jnp.arange(per_dev, dtype=jnp.int32)
    first = here * per_dev + block_index - (WIN_TILES - 1)
    window_tiles = jnp.maximum(first[:, None] + jnp.arange(WIN_TILES, dtype=jnp.int32)[None, :], 0)
    slot_tiles = jnp.concatenate([window_tiles, safe_list, window_tiles[:, :1]], axis=1)
    rows = tile_row(slot_tiles).reshape(-1)

    col = jnp.arange(SLOTS * TILE, dtype=jnp.int32)
    lowest = WINDOW - here * tok_rows - block_index * TILE
    window_cols = (col[None, :] < WIN_TILES * TILE) & (col[None, :] >= lowest[:, None])
    slot_of = jnp.clip(col // TILE - WIN_TILES, 0, SEL - 1)
    sel_cols = (col[None, :] >= WIN_TILES * TILE) & (col[None, :] < (WIN_TILES + SEL) * TILE)
    sel_cols = sel_cols & jnp.take(listed, slot_of, axis=1)
    colmask = (window_cols | sel_cols).astype(jnp.int32).reshape(per_dev, 1, SLOTS * TILE)

    attended = block_attention(rows, queries, colmask, tiles, per_dev, scale)
    return lax.all_to_all(attended, "kvh", split_axis=0, concat_axis=1, tiled=True)


def solution(mesh):
    devices = mesh.devices
    ctx = devices.shape[0]
    z = len({tuple(d.coords)[2] for d in devices[:, 0]})
    z = z if ctx % z == 0 else ctx
    grid = Mesh(devices.reshape(ctx // z, z, devices.shape[1]), ("cy", "cz", "kvh"))
    row = P(("cy", "cz"), "kvh")
    return jax.shard_map(
        per_device,
        mesh=grid,
        in_specs=(row, row, row, P("kvh", ("cy", "cz"), None)),
        out_specs=P(("cy", "cz", "kvh"), None),
        check_vma=False,
    )
```

```python
import functools

import jax
import jax.numpy as jnp
from jax import lax
from jax.experimental import pallas as pl
from jax.experimental.pallas import tpu as pltpu
from jax.sharding import Mesh
from jax.sharding import PartitionSpec as P

TILE = 64
SEL = 16
WINDOW = 256
WIN_TILES = WINDOW // TILE + 1
SLOTS = WIN_TILES + SEL + 1

masked_score = -1e30


def attention_kernel(rows_ref, q_ref, colmask_ref, tiles_hbm, out_ref, kbuf, vbuf, sems, *, per_dev, scale):
    head_size = kbuf.shape[2]
    heads = q_ref.shape[1] // head_size
    keys_per_block = kbuf.shape[1]

    def fetch(b):
        slot = b % 2
        copies = []
        for i in range(SLOTS):
            row = rows_ref[b * SLOTS + i]
            dst = pl.ds(i * TILE, TILE)
            ck = pltpu.make_async_copy(tiles_hbm.at[row], kbuf.at[slot, dst], sems.at[slot, 0, i])
            cv = pltpu.make_async_copy(tiles_hbm.at[row + per_dev], vbuf.at[slot, dst], sems.at[slot, 1, i])
            ck.start()
            cv.start()
            copies += [ck, cv]
        return copies

    r = lax.broadcasted_iota(jnp.int32, (TILE, keys_per_block), 0)
    j = lax.broadcasted_iota(jnp.int32, (TILE, keys_per_block), 1)
    row_ok = (j >= WIN_TILES * TILE) | ((j > r) & (j <= r + WINDOW))
    pending = fetch(0)
    for b in range(per_dev):
        for c in pending:
            c.wait()
        if b + 1 < per_dev:
            pending = fetch(b + 1)
        slot = b % 2
        q = q_ref[pl.ds(b * TILE, TILE), :]
        qs = jnp.concatenate([q[:, h * head_size : (h + 1) * head_size] for h in range(heads)], axis=0)
        s = lax.dot_general(
            qs, kbuf[slot], (((1,), (1,)), ((), ())), preferred_element_type=jnp.float32
        )
        ok = row_ok & (colmask_ref[b] > 0)
        s = jnp.where(ok[None], (s * scale).reshape(heads, TILE, keys_per_block), masked_score)
        s = s.reshape(heads * TILE, keys_per_block)
        peak = jnp.max(s, axis=1, keepdims=True)
        w = jnp.exp(s - peak)
        total = jnp.sum(w, axis=1, keepdims=True)
        num = jnp.dot(w.astype(jnp.bfloat16), vbuf[slot], preferred_element_type=jnp.float32)
        res = (num / total).astype(out_ref.dtype)
        for h in range(heads):
            out_ref[pl.ds(b * TILE, TILE), h * head_size : (h + 1) * head_size] = res[h * TILE : (h + 1) * TILE]


def block_attention(rows, queries, colmask, tiles, per_dev, scale):
    tok_rows, width = queries.shape
    head_size = tiles.shape[2]
    keys_per_block = SLOTS * TILE
    flops = 4 * tok_rows * width * keys_per_block
    vmem = pltpu.MemorySpace.VMEM
    return pl.pallas_call(
        functools.partial(attention_kernel, per_dev=per_dev, scale=scale),
        out_shape=jax.ShapeDtypeStruct((tok_rows, width), queries.dtype),
        in_specs=[
            pl.BlockSpec(memory_space=pltpu.MemorySpace.SMEM),
            pl.BlockSpec(memory_space=vmem),
            pl.BlockSpec(memory_space=vmem),
            pl.BlockSpec(memory_space=pl.ANY),
        ],
        out_specs=pl.BlockSpec(memory_space=vmem),
        scratch_shapes=[
            pltpu.VMEM((2, keys_per_block, head_size), tiles.dtype),
            pltpu.VMEM((2, keys_per_block, head_size), tiles.dtype),
            pltpu.SemaphoreType.DMA((2, 2, SLOTS)),
        ],
        cost_estimate=pl.CostEstimate(
            flops=flops,
            transcendentals=tok_rows * (width // head_size) * keys_per_block,
            bytes_accessed=2 * tok_rows * width * 2 + 2 * per_dev * SLOTS * TILE * head_size * 2,
        ),
    )(rows, queries, colmask, tiles)


def per_device(queries, keys, values, selection):
    tok_rows, head_size = keys.shape
    per_dev = tok_rows // TILE
    n_y = lax.axis_size("cy")
    n_z = lax.axis_size("cz")
    here = lax.axis_index("cy") * n_z + lax.axis_index("cz")
    scale = 1.0 / head_size**0.5

    both = jnp.concatenate([keys, values], axis=0)
    gathered = lax.all_gather(both, "cy", axis=0, tiled=False)
    gathered = lax.all_gather(gathered, "cz", axis=0, tiled=False)
    tiles = gathered.reshape(n_z * n_y * 2 * per_dev, TILE, head_size)

    def tile_row(tile_id):
        owner = tile_id // per_dev
        return (((owner % n_z) * n_y + owner // n_z) * 2) * per_dev + tile_id % per_dev

    lists = selection[0]
    listed = lists >= 0
    safe_list = jnp.maximum(lists, 0)
    block_index = jnp.arange(per_dev, dtype=jnp.int32)
    first = here * per_dev + block_index - (WIN_TILES - 1)
    window_tiles = jnp.maximum(first[:, None] + jnp.arange(WIN_TILES, dtype=jnp.int32)[None, :], 0)
    slot_tiles = jnp.concatenate([window_tiles, safe_list, window_tiles[:, :1]], axis=1)
    rows = tile_row(slot_tiles).reshape(-1)

    col = jnp.arange(SLOTS * TILE, dtype=jnp.int32)
    lowest = WINDOW - here * tok_rows - block_index * TILE
    window_cols = (col[None, :] < WIN_TILES * TILE) & (col[None, :] >= lowest[:, None])
    slot_of = jnp.clip(col // TILE - WIN_TILES, 0, SEL - 1)
    sel_cols = (col[None, :] >= WIN_TILES * TILE) & (col[None, :] < (WIN_TILES + SEL) * TILE)
    sel_cols = sel_cols & jnp.take(listed, slot_of, axis=1)
    colmask = (window_cols | sel_cols).astype(jnp.int32).reshape(per_dev, 1, SLOTS * TILE)

    attended = block_attention(rows, queries, colmask, tiles, per_dev, scale)
    return lax.all_to_all(attended, "kvh", split_axis=0, concat_axis=1, tiled=True)


def solution(mesh):
    devices = mesh.devices
    ctx = devices.shape[0]
    z = len({tuple(d.coords)[2] for d in devices[:, 0]})
    z = z if ctx % z == 0 else ctx
    grid = Mesh(devices.reshape(ctx // z, z, devices.shape[1]), ("cy", "cz", "kvh"))
    row = P(("cy", "cz"), "kvh")
    return jax.shard_map(
        per_device,
        mesh=grid,
        in_specs=(row, row, row, P("kvh", ("cy", "cz"), None)),
        out_specs=P(("cy", "cz", "kvh"), None),
        check_vma=False,
    )
```

```python
import functools

import jax
import jax.numpy as jnp
from jax import lax
from jax.experimental import pallas as pl
from jax.experimental.pallas import tpu as pltpu
from jax.sharding import Mesh
from jax.sharding import PartitionSpec as P

TILE = 64
SEL = 16
WINDOW = 256
WIN_COLS = WINDOW + 2 * TILE
SEL_COLS = SEL * TILE

masked_score = -1e30


def attention_kernel(
    rows_ref, prev_ref, q_ref, keys_ref, values_ref, colmask_ref, tiles_hbm, out_ref,
    selbuf, prevbuf, wink, winv, sems, prev_sem, *, per_dev, scale,
):
    head_size = keys_ref.shape[1]
    tok_rows = keys_ref.shape[0]
    heads = q_ref.shape[1] // head_size

    def fetch(b):
        slot = b % 2
        copies = []
        for i in range(SEL):
            cp = pltpu.make_async_copy(tiles_hbm.at[rows_ref[b * SEL + i]], selbuf.at[slot, i], sems.at[slot, i])
            cp.start()
            copies.append(cp)
        return copies

    prev_copy = pltpu.make_async_copy(tiles_hbm.at[pl.ds(prev_ref[0], per_dev)], prevbuf, prev_sem.at[0])
    prev_copy.start()
    pending = fetch(0)
    wink[pl.ds(tok_rows, tok_rows), :] = keys_ref[...]
    winv[pl.ds(tok_rows, tok_rows), :] = values_ref[...]
    pad = wink.shape[0] - 2 * tok_rows
    wink[pl.ds(2 * tok_rows, pad), :] = jnp.zeros((pad, head_size), wink.dtype)
    winv[pl.ds(2 * tok_rows, pad), :] = jnp.zeros((pad, head_size), winv.dtype)
    prev_copy.wait()
    wink[pl.ds(0, tok_rows), :] = prevbuf[:, 0].reshape(tok_rows, head_size)
    winv[pl.ds(0, tok_rows), :] = prevbuf[:, 1].reshape(tok_rows, head_size)

    r = lax.broadcasted_iota(jnp.int32, (TILE, WIN_COLS), 0)
    j = lax.broadcasted_iota(jnp.int32, (TILE, WIN_COLS), 1)
    in_window = (j > r) & (j <= r + WINDOW)
    dims = (((1,), (1,)), ((), ()))
    for b in range(per_dev):
        for c in pending:
            c.wait()
        if b + 1 < per_dev:
            pending = fetch(b + 1)
        slot = b % 2
        q = q_ref[pl.ds(b * TILE, TILE), :]
        qs = jnp.concatenate([q[:, h * head_size : (h + 1) * head_size] for h in range(heads)], axis=0)
        k_win = wink[pl.ds(b * TILE, WIN_COLS), :]
        v_win = winv[pl.ds(b * TILE, WIN_COLS), :]
        k_sel = selbuf[slot, :, 0].reshape(SEL_COLS, head_size)
        v_sel = selbuf[slot, :, 1].reshape(SEL_COLS, head_size)
        mask = colmask_ref[b]
        win_ok = in_window & (mask[:, :WIN_COLS] > 0)
        sel_ok = mask[:, WIN_COLS:] > 0
        s_win = lax.dot_general(qs, k_win, dims, preferred_element_type=jnp.float32) * scale
        s_sel = lax.dot_general(qs, k_sel, dims, preferred_element_type=jnp.float32) * scale
        s_win = jnp.where(win_ok[None], s_win.reshape(heads, TILE, WIN_COLS), masked_score)
        s_win = s_win.reshape(heads * TILE, WIN_COLS)
        s_sel = jnp.where(sel_ok, s_sel, masked_score)
        peak = jnp.maximum(jnp.max(s_win, axis=1, keepdims=True), jnp.max(s_sel, axis=1, keepdims=True))
        w_win = jnp.exp(s_win - peak)
        w_sel = jnp.exp(s_sel - peak)
        total = jnp.sum(w_win, axis=1, keepdims=True) + jnp.sum(w_sel, axis=1, keepdims=True)
        num = jnp.dot(w_win.astype(jnp.bfloat16), v_win, preferred_element_type=jnp.float32)
        num = num + jnp.dot(w_sel.astype(jnp.bfloat16), v_sel, preferred_element_type=jnp.float32)
        res = (num / total).astype(out_ref.dtype)
        for h in range(heads):
            out_ref[pl.ds(b * TILE, TILE), h * head_size : (h + 1) * head_size] = res[h * TILE : (h + 1) * TILE]


def block_attention(rows, prev, queries, keys, values, colmask, tiles, per_dev, scale):
    tok_rows, width = queries.shape
    head_size = keys.shape[1]
    keys_per_block = WIN_COLS + SEL_COLS
    vmem = pltpu.MemorySpace.VMEM
    smem = pltpu.MemorySpace.SMEM
    return pl.pallas_call(
        functools.partial(attention_kernel, per_dev=per_dev, scale=scale),
        out_shape=jax.ShapeDtypeStruct((tok_rows, width), queries.dtype),
        in_specs=[
            pl.BlockSpec(memory_space=smem),
            pl.BlockSpec(memory_space=smem),
            pl.BlockSpec(memory_space=vmem),
            pl.BlockSpec(memory_space=vmem),
            pl.BlockSpec(memory_space=vmem),
            pl.BlockSpec(memory_space=vmem),
            pl.BlockSpec(memory_space=pl.ANY),
        ],
        out_specs=pl.BlockSpec(memory_space=vmem),
        scratch_shapes=[
            pltpu.VMEM((2, SEL, 2, TILE, head_size), tiles.dtype),
            pltpu.VMEM((per_dev, 2, TILE, head_size), tiles.dtype),
            pltpu.VMEM((2 * tok_rows + TILE, head_size), tiles.dtype),
            pltpu.VMEM((2 * tok_rows + TILE, head_size), tiles.dtype),
            pltpu.SemaphoreType.DMA((2, SEL)),
            pltpu.SemaphoreType.DMA((1,)),
        ],
        cost_estimate=pl.CostEstimate(
            flops=4 * tok_rows * width * keys_per_block,
            transcendentals=tok_rows * (width // head_size) * keys_per_block,
            bytes_accessed=2 * tok_rows * width * 2 + 2 * per_dev * SEL_COLS * head_size * 2,
        ),
    )(rows, prev, queries, keys, values, colmask, tiles)


def device_attention(queries, keys, values, lists, tiles, here, n_y, n_z):
    tok_rows, head_size = keys.shape
    per_dev = tok_rows // TILE
    scale = 1.0 / head_size**0.5

    def tile_index(tile_id):
        owner = tile_id // per_dev
        return ((owner % n_z) * n_y + owner // n_z) * per_dev + tile_id % per_dev

    listed = lists >= 0
    rows = tile_index(jnp.maximum(lists, 0)).reshape(-1).astype(jnp.int32)
    prev = tile_index(jnp.maximum(here - 1, 0) * per_dev).reshape(1).astype(jnp.int32)

    block_index = jnp.arange(per_dev, dtype=jnp.int32)
    win_col = jnp.arange(WIN_COLS, dtype=jnp.int32)
    lowest = WINDOW - here * tok_rows - block_index * TILE
    win_flags = (win_col[None, :] < WINDOW + TILE) & (win_col[None, :] >= lowest[:, None])
    sel_flags = jnp.repeat(listed, TILE, axis=1)
    colmask = jnp.concatenate([win_flags, sel_flags], axis=1).astype(jnp.int32)
    colmask = colmask.reshape(per_dev, 1, WIN_COLS + SEL_COLS)
    return block_attention(rows, prev, queries, keys, values, colmask, tiles, per_dev, scale)


def per_device(queries, keys, values, selection):
    tok_rows, head_size = keys.shape
    per_dev = tok_rows // TILE
    n_y = lax.axis_size("cy")
    n_z = lax.axis_size("cz")
    here = lax.axis_index("cy") * n_z + lax.axis_index("cz")

    both = jnp.stack(
        [keys.reshape(per_dev, TILE, head_size), values.reshape(per_dev, TILE, head_size)], axis=1
    )
    gathered = lax.all_gather(both, "cy", axis=0, tiled=False)
    gathered = lax.all_gather(gathered, "cz", axis=0, tiled=False)
    tiles = gathered.reshape(n_z * n_y * per_dev, 2, TILE, head_size)
    attended = device_attention(queries, keys, values, selection[0], tiles, here, n_y, n_z)
    return lax.all_to_all(attended, "kvh", split_axis=0, concat_axis=1, tiled=True)


def solution(mesh):
    devices = mesh.devices
    ctx = devices.shape[0]
    z = len({tuple(d.coords)[2] for d in devices[:, 0]})
    z = z if ctx % z == 0 else ctx
    grid = Mesh(devices.reshape(ctx // z, z, devices.shape[1]), ("cy", "cz", "kvh"))
    row = P(("cy", "cz"), "kvh")
    return jax.shard_map(
        per_device,
        mesh=grid,
        in_specs=(row, row, row, P("kvh", ("cy", "cz"), None)),
        out_specs=P(("cy", "cz", "kvh"), None),
        check_vma=False,
    )
```

```python
import functools

import jax
import jax.numpy as jnp
from jax import lax
from jax.experimental import pallas as pl
from jax.experimental.pallas import tpu as pltpu
from jax.sharding import Mesh
from jax.sharding import PartitionSpec as P

TILE = 64
SEL = 16
WINDOW = 256
WIN_COLS = WINDOW + 2 * TILE
SEL_COLS = SEL * TILE

masked_score = -1e30


def window_kernel(q_ref, wink_ref, winv_ref, colmask_ref, acc_ref, peak_ref, total_ref, *, per_dev, scale):
    head_size = wink_ref.shape[1]
    heads = q_ref.shape[1] // head_size
    r = lax.broadcasted_iota(jnp.int32, (TILE, WIN_COLS), 0)
    j = lax.broadcasted_iota(jnp.int32, (TILE, WIN_COLS), 1)
    in_window = (j > r) & (j <= r + WINDOW)
    dims = (((1,), (1,)), ((), ()))
    for b in range(per_dev):
        q = q_ref[pl.ds(b * TILE, TILE), :]
        qs = jnp.concatenate([q[:, h * head_size : (h + 1) * head_size] for h in range(heads)], axis=0)
        k_win = wink_ref[pl.ds(b * TILE, WIN_COLS), :]
        v_win = winv_ref[pl.ds(b * TILE, WIN_COLS), :]
        win_ok = in_window & (colmask_ref[b] > 0)
        s_win = lax.dot_general(qs, k_win, dims, preferred_element_type=jnp.float32) * scale
        s_win = jnp.where(win_ok[None], s_win.reshape(heads, TILE, WIN_COLS), masked_score)
        s_win = s_win.reshape(heads * TILE, WIN_COLS)
        peak = jnp.max(s_win, axis=1, keepdims=True)
        w_win = jnp.exp(s_win - peak)
        total_ref[b] = jnp.sum(w_win, axis=1, keepdims=True)
        peak_ref[b] = peak
        acc_ref[b] = jnp.dot(w_win.astype(jnp.bfloat16), v_win, preferred_element_type=jnp.float32)


def window_attention(queries, wink, winv, colmask, per_dev, scale):
    tok_rows, width = queries.shape
    head_size = wink.shape[1]
    rows = tok_rows * (width // head_size) // per_dev
    vmem = pltpu.MemorySpace.VMEM
    return pl.pallas_call(
        functools.partial(window_kernel, per_dev=per_dev, scale=scale),
        out_shape=(
            jax.ShapeDtypeStruct((per_dev, rows, head_size), jnp.float32),
            jax.ShapeDtypeStruct((per_dev, rows, 1), jnp.float32),
            jax.ShapeDtypeStruct((per_dev, rows, 1), jnp.float32),
        ),
        in_specs=[pl.BlockSpec(memory_space=vmem)] * 4,
        out_specs=tuple([pl.BlockSpec(memory_space=vmem)] * 3),
        cost_estimate=pl.CostEstimate(
            flops=4 * tok_rows * width * WIN_COLS,
            transcendentals=tok_rows * (width // head_size) * WIN_COLS,
            bytes_accessed=tok_rows * width * 2 + per_dev * rows * (head_size + 2) * 4,
        ),
    )(queries, wink, winv, colmask)


def attention_kernel(
    rows_ref, q_ref, colmask_ref, acc_ref, peak_ref, total_ref, tiles_hbm, out_ref, selbuf, sems, *, per_dev, scale,
):
    head_size = tiles_hbm.shape[3]
    heads = q_ref.shape[1] // head_size

    def fetch(b):
        slot = b % 2
        copies = []
        for i in range(SEL):
            cp = pltpu.make_async_copy(tiles_hbm.at[rows_ref[b * SEL + i]], selbuf.at[slot, i], sems.at[slot, i])
            cp.start()
            copies.append(cp)
        return copies

    pending = fetch(0)
    dims = (((1,), (1,)), ((), ()))
    for b in range(per_dev):
        for c in pending:
            c.wait()
        if b + 1 < per_dev:
            pending = fetch(b + 1)
        slot = b % 2
        q = q_ref[pl.ds(b * TILE, TILE), :]
        qs = jnp.concatenate([q[:, h * head_size : (h + 1) * head_size] for h in range(heads)], axis=0)
        k_sel = selbuf[slot, :, 0].reshape(SEL_COLS, head_size)
        v_sel = selbuf[slot, :, 1].reshape(SEL_COLS, head_size)
        sel_ok = colmask_ref[b] > 0
        s_sel = lax.dot_general(qs, k_sel, dims, preferred_element_type=jnp.float32) * scale
        s_sel = jnp.where(sel_ok, s_sel, masked_score)
        win_peak = peak_ref[b]
        peak = jnp.maximum(win_peak, jnp.max(s_sel, axis=1, keepdims=True))
        w_sel = jnp.exp(s_sel - peak)
        rescale = jnp.exp(win_peak - peak)
        total = total_ref[b] * rescale + jnp.sum(w_sel, axis=1, keepdims=True)
        num = acc_ref[b] * rescale
        num = num + jnp.dot(w_sel.astype(jnp.bfloat16), v_sel, preferred_element_type=jnp.float32)
        res = (num / total).astype(out_ref.dtype)
        for h in range(heads):
            out_ref[pl.ds(b * TILE, TILE), h * head_size : (h + 1) * head_size] = res[h * TILE : (h + 1) * TILE]


def block_attention(rows, queries, colmask, acc, peak, total, tiles, per_dev, scale):
    tok_rows, width = queries.shape
    head_size = tiles.shape[3]
    vmem = pltpu.MemorySpace.VMEM
    smem = pltpu.MemorySpace.SMEM
    return pl.pallas_call(
        functools.partial(attention_kernel, per_dev=per_dev, scale=scale),
        out_shape=jax.ShapeDtypeStruct((tok_rows, width), queries.dtype),
        in_specs=[pl.BlockSpec(memory_space=smem)]
        + [pl.BlockSpec(memory_space=vmem)] * 5
        + [pl.BlockSpec(memory_space=pl.ANY)],
        out_specs=pl.BlockSpec(memory_space=vmem),
        scratch_shapes=[
            pltpu.VMEM((2, SEL, 2, TILE, head_size), tiles.dtype),
            pltpu.SemaphoreType.DMA((2, SEL)),
        ],
        cost_estimate=pl.CostEstimate(
            flops=4 * tok_rows * width * SEL_COLS,
            transcendentals=tok_rows * (width // head_size) * SEL_COLS,
            bytes_accessed=2 * tok_rows * width * 2 + 2 * per_dev * SEL_COLS * head_size * 2,
        ),
    )(rows, queries, colmask, acc, peak, total, tiles)


def window_part(queries, keys, values, prev_keys, prev_values, here):
    tok_rows, head_size = keys.shape
    per_dev = tok_rows // TILE
    scale = 1.0 / head_size**0.5
    pad = jnp.zeros((TILE, head_size), keys.dtype)
    wink = jnp.concatenate([prev_keys, keys, pad], axis=0)
    winv = jnp.concatenate([prev_values, values, pad], axis=0)
    block_index = jnp.arange(per_dev, dtype=jnp.int32)
    win_col = jnp.arange(WIN_COLS, dtype=jnp.int32)
    lowest = WINDOW - here * tok_rows - block_index * TILE
    win_flags = (win_col[None, :] < WINDOW + TILE) & (win_col[None, :] >= lowest[:, None])
    win_flags = win_flags.astype(jnp.int32).reshape(per_dev, 1, WIN_COLS)
    return window_attention(queries, wink, winv, win_flags, per_dev, scale)


def selected_part(queries, lists, tiles, window, n_y, n_z):
    tok_rows, width = queries.shape
    head_size = tiles.shape[3]
    per_dev = tok_rows // TILE
    scale = 1.0 / head_size**0.5

    def tile_index(tile_id):
        owner = tile_id // per_dev
        return ((owner % n_z) * n_y + owner // n_z) * per_dev + tile_id % per_dev

    rows = tile_index(jnp.maximum(lists, 0)).reshape(-1).astype(jnp.int32)
    sel_flags = jnp.repeat(lists >= 0, TILE, axis=1).astype(jnp.int32).reshape(per_dev, 1, SEL_COLS)
    acc, peak, total = window
    return block_attention(rows, queries, sel_flags, acc, peak, total, tiles, per_dev, scale)


def per_device(queries, keys, values, selection):
    tok_rows, head_size = keys.shape
    per_dev = tok_rows // TILE
    n_y = lax.axis_size("cy")
    n_z = lax.axis_size("cz")
    here = lax.axis_index("cy") * n_z + lax.axis_index("cz")

    both = jnp.stack(
        [keys.reshape(per_dev, TILE, head_size), values.reshape(per_dev, TILE, head_size)], axis=1
    )
    gathered = lax.all_gather(both, "cy", axis=0, tiled=False)
    gathered = lax.all_gather(gathered, "cz", axis=0, tiled=False)
    tiles = gathered.reshape(n_z * n_y * per_dev, 2, TILE, head_size)
    count = n_y * n_z
    earlier = [(i, i + 1) for i in range(count - 1)]
    prev_keys, prev_values = lax.ppermute((keys, values), ("cy", "cz"), earlier)
    window = window_part(queries, keys, values, prev_keys, prev_values, here)
    attended = selected_part(queries, selection[0], tiles, window, n_y, n_z)
    return lax.all_to_all(attended, "kvh", split_axis=0, concat_axis=1, tiled=True)


def solution(mesh):
    devices = mesh.devices
    ctx = devices.shape[0]
    z = len({tuple(d.coords)[2] for d in devices[:, 0]})
    z = z if ctx % z == 0 else ctx
    grid = Mesh(devices.reshape(ctx // z, z, devices.shape[1]), ("cy", "cz", "kvh"))
    row = P(("cy", "cz"), "kvh")
    return jax.shard_map(
        per_device,
        mesh=grid,
        in_specs=(row, row, row, P("kvh", ("cy", "cz"), None)),
        out_specs=P(("cy", "cz", "kvh"), None),
        check_vma=False,
    )
```

```python
import functools

import jax
import jax.numpy as jnp
from jax import lax
from jax.experimental import pallas as pl
from jax.experimental.pallas import tpu as pltpu
from jax.sharding import Mesh
from jax.sharding import PartitionSpec as P

TILE = 64
SEL = 16
WINDOW = 256
WIN_COLS = WINDOW + 2 * TILE
SEL_COLS = SEL * TILE

masked_score = -1e30


def attention_kernel(
    rows_ref, prev_ref, q_ref, keys_ref, values_ref, colmask_ref, tiles_hbm, out_ref,
    selbuf, prevbuf, wink, winv, sems, prev_sem, *, per_dev, scale,
):
    head_size = keys_ref.shape[1]
    tok_rows = keys_ref.shape[0]
    heads = q_ref.shape[1] // head_size

    def fetch(b):
        slot = b % 2
        copies = []
        for i in range(SEL):
            cp = pltpu.make_async_copy(tiles_hbm.at[rows_ref[b * SEL + i]], selbuf.at[slot, i], sems.at[slot, i])
            cp.start()
            copies.append(cp)
        return copies

    prev_copy = pltpu.make_async_copy(tiles_hbm.at[pl.ds(prev_ref[0], per_dev)], prevbuf, prev_sem.at[0])
    prev_copy.start()
    pending = fetch(0)
    wink[pl.ds(tok_rows, tok_rows), :] = keys_ref[...]
    winv[pl.ds(tok_rows, tok_rows), :] = values_ref[...]
    pad = wink.shape[0] - 2 * tok_rows
    wink[pl.ds(2 * tok_rows, pad), :] = jnp.zeros((pad, head_size), wink.dtype)
    winv[pl.ds(2 * tok_rows, pad), :] = jnp.zeros((pad, head_size), winv.dtype)
    prev_copy.wait()
    wink[pl.ds(0, tok_rows), :] = prevbuf[:, 0].reshape(tok_rows, head_size)
    winv[pl.ds(0, tok_rows), :] = prevbuf[:, 1].reshape(tok_rows, head_size)

    r = lax.broadcasted_iota(jnp.int32, (TILE, WIN_COLS), 0)
    j = lax.broadcasted_iota(jnp.int32, (TILE, WIN_COLS), 1)
    in_window = (j > r) & (j <= r + WINDOW)
    dims = (((1,), (1,)), ((), ()))
    for b in range(per_dev):
        for c in pending:
            c.wait()
        if b + 1 < per_dev:
            pending = fetch(b + 1)
        slot = b % 2
        q = q_ref[pl.ds(b * TILE, TILE), :]
        qs = jnp.concatenate([q[:, h * head_size : (h + 1) * head_size] for h in range(heads)], axis=0)
        k_win = wink[pl.ds(b * TILE, WIN_COLS), :]
        v_win = winv[pl.ds(b * TILE, WIN_COLS), :]
        k_sel = selbuf[slot, :, 0].reshape(SEL_COLS, head_size)
        v_sel = selbuf[slot, :, 1].reshape(SEL_COLS, head_size)
        mask = colmask_ref[b]
        win_ok = in_window & (mask[:, :WIN_COLS] > 0)
        sel_ok = mask[:, WIN_COLS:] > 0
        s_win = lax.dot_general(qs, k_win, dims, preferred_element_type=jnp.float32) * scale
        s_sel = lax.dot_general(qs, k_sel, dims, preferred_element_type=jnp.float32) * scale
        s_win = jnp.where(win_ok[None], s_win.reshape(heads, TILE, WIN_COLS), masked_score)
        s_win = s_win.reshape(heads * TILE, WIN_COLS)
        s_sel = jnp.where(sel_ok, s_sel, masked_score)
        peak = jnp.maximum(jnp.max(s_win, axis=1, keepdims=True), jnp.max(s_sel, axis=1, keepdims=True))
        w_win = jnp.exp(s_win - peak)
        w_sel = jnp.exp(s_sel - peak)
        total = jnp.sum(w_win, axis=1, keepdims=True) + jnp.sum(w_sel, axis=1, keepdims=True)
        num = jnp.dot(w_win.astype(jnp.bfloat16), v_win, preferred_element_type=jnp.float32)
        num = num + jnp.dot(w_sel.astype(jnp.bfloat16), v_sel, preferred_element_type=jnp.float32)
        res = (num / total).astype(out_ref.dtype)
        for h in range(heads):
            out_ref[pl.ds(b * TILE, TILE), h * head_size : (h + 1) * head_size] = res[h * TILE : (h + 1) * TILE]


def block_attention(rows, prev, queries, keys, values, colmask, tiles, per_dev, scale):
    tok_rows, width = queries.shape
    head_size = keys.shape[1]
    keys_per_block = WIN_COLS + SEL_COLS
    vmem = pltpu.MemorySpace.VMEM
    smem = pltpu.MemorySpace.SMEM
    return pl.pallas_call(
        functools.partial(attention_kernel, per_dev=per_dev, scale=scale),
        out_shape=jax.ShapeDtypeStruct((tok_rows, width), queries.dtype),
        in_specs=[
            pl.BlockSpec(memory_space=smem),
            pl.BlockSpec(memory_space=smem),
            pl.BlockSpec(memory_space=vmem),
            pl.BlockSpec(memory_space=vmem),
            pl.BlockSpec(memory_space=vmem),
            pl.BlockSpec(memory_space=vmem),
            pl.BlockSpec(memory_space=pl.ANY),
        ],
        out_specs=pl.BlockSpec(memory_space=vmem),
        scratch_shapes=[
            pltpu.VMEM((2, SEL, 2, TILE, head_size), tiles.dtype),
            pltpu.VMEM((per_dev, 2, TILE, head_size), tiles.dtype),
            pltpu.VMEM((2 * tok_rows + TILE, head_size), tiles.dtype),
            pltpu.VMEM((2 * tok_rows + TILE, head_size), tiles.dtype),
            pltpu.SemaphoreType.DMA((2, SEL)),
            pltpu.SemaphoreType.DMA((1,)),
        ],
        cost_estimate=pl.CostEstimate(
            flops=4 * tok_rows * width * keys_per_block,
            transcendentals=tok_rows * (width // head_size) * keys_per_block,
            bytes_accessed=2 * tok_rows * width * 2 + 2 * per_dev * SEL_COLS * head_size * 2,
        ),
    )(rows, prev, queries, keys, values, colmask, tiles)


def device_attention(queries, keys, values, lists, tiles, here, n_y, n_z):
    tok_rows, head_size = keys.shape
    per_dev = tok_rows // TILE
    scale = 1.0 / head_size**0.5

    def tile_index(tile_id):
        owner = tile_id // per_dev
        return ((owner % n_z) * n_y + owner // n_z) * per_dev + tile_id % per_dev

    listed = lists >= 0
    rows = tile_index(jnp.maximum(lists, 0)).reshape(-1).astype(jnp.int32)
    prev = tile_index(jnp.maximum(here - 1, 0) * per_dev).reshape(1).astype(jnp.int32)

    block_index = jnp.arange(per_dev, dtype=jnp.int32)
    win_col = jnp.arange(WIN_COLS, dtype=jnp.int32)
    lowest = WINDOW - here * tok_rows - block_index * TILE
    win_flags = (win_col[None, :] < WINDOW + TILE) & (win_col[None, :] >= lowest[:, None])
    sel_flags = jnp.repeat(listed, TILE, axis=1)
    colmask = jnp.concatenate([win_flags, sel_flags], axis=1).astype(jnp.int32)
    colmask = colmask.reshape(per_dev, 1, WIN_COLS + SEL_COLS)
    return block_attention(rows, prev, queries, keys, values, colmask, tiles, per_dev, scale)


def per_device(queries, keys, values, selection):
    tok_rows, head_size = keys.shape
    per_dev = tok_rows // TILE
    n_y = lax.axis_size("cy")
    n_z = lax.axis_size("cz")
    here = lax.axis_index("cy") * n_z + lax.axis_index("cz")

    both = jnp.stack(
        [keys.reshape(per_dev, TILE, head_size), values.reshape(per_dev, TILE, head_size)], axis=1
    )
    copies = jnp.broadcast_to(both[None], (n_y,) + both.shape)
    gathered = lax.all_to_all(copies, "cy", 0, 0, tiled=False)
    gathered = lax.all_gather(gathered, "cz", axis=0, tiled=False)
    tiles = gathered.reshape(n_z * n_y * per_dev, 2, TILE, head_size)
    attended = device_attention(queries, keys, values, selection[0], tiles, here, n_y, n_z)
    return lax.all_to_all(attended, "kvh", split_axis=0, concat_axis=1, tiled=True)


def solution(mesh):
    devices = mesh.devices
    ctx = devices.shape[0]
    z = len({tuple(d.coords)[2] for d in devices[:, 0]})
    z = z if ctx % z == 0 else ctx
    grid = Mesh(devices.reshape(ctx // z, z, devices.shape[1]), ("cy", "cz", "kvh"))
    row = P(("cy", "cz"), "kvh")
    return jax.shard_map(
        per_device,
        mesh=grid,
        in_specs=(row, row, row, P("kvh", ("cy", "cz"), None)),
        out_specs=P(("cy", "cz", "kvh"), None),
        check_vma=False,
    )
```

```python
import functools

import jax
import jax.numpy as jnp
from jax import lax
from jax.experimental import pallas as pl
from jax.experimental.pallas import tpu as pltpu
from jax.sharding import Mesh
from jax.sharding import PartitionSpec as P

TILE = 64
SEL = 16
WINDOW = 256
WIN_COLS = WINDOW + 2 * TILE
SEL_COLS = SEL * TILE

masked_score = -1e30


def attention_kernel(
    rows_ref, ring_rows_ref, from_ring_ref, prev_ref, q_ref, keys_ref, values_ref, colmask_ref, tiles_hbm, ring_hbm,
    out_ref, selbuf, prevbuf, wink, winv, sems, prev_sem, *, per_dev, scale,
):
    head_size = keys_ref.shape[1]
    tok_rows = keys_ref.shape[0]
    heads = q_ref.shape[1] // head_size

    def fetch(b):
        slot = b % 2
        copies = []
        for i in range(SEL):
            k = b * SEL + i
            cp = pltpu.make_async_copy(tiles_hbm.at[rows_ref[k]], selbuf.at[slot, i], sems.at[slot, i])
            cr = pltpu.make_async_copy(ring_hbm.at[ring_rows_ref[k]], selbuf.at[slot, i], sems.at[slot, i])
            pl.when(from_ring_ref[k] == 0)(cp.start)
            pl.when(from_ring_ref[k] != 0)(cr.start)
            copies.append(cp)
        return copies

    prev_copy = pltpu.make_async_copy(tiles_hbm.at[pl.ds(prev_ref[0], per_dev)], prevbuf, prev_sem.at[0])
    prev_ring = pltpu.make_async_copy(ring_hbm.at[pl.ds(prev_ref[1], per_dev)], prevbuf, prev_sem.at[0])
    pl.when(prev_ref[2] == 0)(prev_copy.start)
    pl.when(prev_ref[2] != 0)(prev_ring.start)
    pending = fetch(0)
    wink[pl.ds(tok_rows, tok_rows), :] = keys_ref[...]
    winv[pl.ds(tok_rows, tok_rows), :] = values_ref[...]
    pad = wink.shape[0] - 2 * tok_rows
    wink[pl.ds(2 * tok_rows, pad), :] = jnp.zeros((pad, head_size), wink.dtype)
    winv[pl.ds(2 * tok_rows, pad), :] = jnp.zeros((pad, head_size), winv.dtype)
    prev_copy.wait()
    wink[pl.ds(0, tok_rows), :] = prevbuf[:, 0].reshape(tok_rows, head_size)
    winv[pl.ds(0, tok_rows), :] = prevbuf[:, 1].reshape(tok_rows, head_size)

    r = lax.broadcasted_iota(jnp.int32, (TILE, WIN_COLS), 0)
    j = lax.broadcasted_iota(jnp.int32, (TILE, WIN_COLS), 1)
    in_window = (j > r) & (j <= r + WINDOW)
    dims = (((1,), (1,)), ((), ()))
    for b in range(per_dev):
        for c in pending:
            c.wait()
        if b + 1 < per_dev:
            pending = fetch(b + 1)
        slot = b % 2
        q = q_ref[pl.ds(b * TILE, TILE), :]
        qs = jnp.concatenate([q[:, h * head_size : (h + 1) * head_size] for h in range(heads)], axis=0)
        k_win = wink[pl.ds(b * TILE, WIN_COLS), :]
        v_win = winv[pl.ds(b * TILE, WIN_COLS), :]
        k_sel = selbuf[slot, :, 0].reshape(SEL_COLS, head_size)
        v_sel = selbuf[slot, :, 1].reshape(SEL_COLS, head_size)
        mask = colmask_ref[b]
        win_ok = in_window & (mask[:, :WIN_COLS] > 0)
        sel_ok = mask[:, WIN_COLS:] > 0
        s_win = lax.dot_general(qs, k_win, dims, preferred_element_type=jnp.float32) * scale
        s_sel = lax.dot_general(qs, k_sel, dims, preferred_element_type=jnp.float32) * scale
        s_win = jnp.where(win_ok[None], s_win.reshape(heads, TILE, WIN_COLS), masked_score)
        s_win = s_win.reshape(heads * TILE, WIN_COLS)
        s_sel = jnp.where(sel_ok, s_sel, masked_score)
        peak = jnp.maximum(jnp.max(s_win, axis=1, keepdims=True), jnp.max(s_sel, axis=1, keepdims=True))
        w_win = jnp.exp(s_win - peak)
        w_sel = jnp.exp(s_sel - peak)
        total = jnp.sum(w_win, axis=1, keepdims=True) + jnp.sum(w_sel, axis=1, keepdims=True)
        num = jnp.dot(w_win.astype(jnp.bfloat16), v_win, preferred_element_type=jnp.float32)
        num = num + jnp.dot(w_sel.astype(jnp.bfloat16), v_sel, preferred_element_type=jnp.float32)
        res = (num / total).astype(out_ref.dtype)
        for h in range(heads):
            out_ref[pl.ds(b * TILE, TILE), h * head_size : (h + 1) * head_size] = res[h * TILE : (h + 1) * TILE]


def block_attention(rows, ring_rows, from_ring, prev, queries, keys, values, colmask, tiles, ring, per_dev, scale):
    tok_rows, width = queries.shape
    head_size = keys.shape[1]
    keys_per_block = WIN_COLS + SEL_COLS
    vmem = pltpu.MemorySpace.VMEM
    smem = pltpu.MemorySpace.SMEM
    return pl.pallas_call(
        functools.partial(attention_kernel, per_dev=per_dev, scale=scale),
        out_shape=jax.ShapeDtypeStruct((tok_rows, width), queries.dtype),
        in_specs=[
            pl.BlockSpec(memory_space=smem),
            pl.BlockSpec(memory_space=smem),
            pl.BlockSpec(memory_space=smem),
            pl.BlockSpec(memory_space=smem),
            pl.BlockSpec(memory_space=vmem),
            pl.BlockSpec(memory_space=vmem),
            pl.BlockSpec(memory_space=vmem),
            pl.BlockSpec(memory_space=vmem),
            pl.BlockSpec(memory_space=pl.ANY),
            pl.BlockSpec(memory_space=pl.ANY),
        ],
        out_specs=pl.BlockSpec(memory_space=vmem),
        scratch_shapes=[
            pltpu.VMEM((2, SEL, 2, TILE, head_size), tiles.dtype),
            pltpu.VMEM((per_dev, 2, TILE, head_size), tiles.dtype),
            pltpu.VMEM((2 * tok_rows + TILE, head_size), tiles.dtype),
            pltpu.VMEM((2 * tok_rows + TILE, head_size), tiles.dtype),
            pltpu.SemaphoreType.DMA((2, SEL)),
            pltpu.SemaphoreType.DMA((1,)),
        ],
        cost_estimate=pl.CostEstimate(
            flops=4 * tok_rows * width * keys_per_block,
            transcendentals=tok_rows * (width // head_size) * keys_per_block,
            bytes_accessed=2 * tok_rows * width * 2 + 2 * per_dev * SEL_COLS * head_size * 2,
        ),
    )(rows, ring_rows, from_ring, prev, queries, keys, values, colmask, tiles, ring)


def device_attention(queries, keys, values, lists, tiles, ring, here, n_y, n_z):
    tok_rows, head_size = keys.shape
    per_dev = tok_rows // TILE
    scale = 1.0 / head_size**0.5
    my_z = here % n_z

    def locate(tile_id):
        owner = tile_id // per_dev
        y, z = owner // n_z, owner % n_z
        in_ring = y == n_y - 1
        row = ((z * (n_y - 1) + jnp.minimum(y, n_y - 2)) * per_dev + tile_id % per_dev).astype(jnp.int32)
        ring_row = (((my_z - z) % n_z) * per_dev + tile_id % per_dev).astype(jnp.int32)
        return row, ring_row, in_ring.astype(jnp.int32)

    listed = lists >= 0
    rows, ring_rows, from_ring = (a.reshape(-1) for a in locate(jnp.maximum(lists, 0)))
    prev_row, prev_ring_row, prev_in_ring = locate(jnp.maximum(here - 1, 0) * per_dev)
    prev = jnp.stack([prev_row, prev_ring_row, prev_in_ring]).astype(jnp.int32)

    block_index = jnp.arange(per_dev, dtype=jnp.int32)
    win_col = jnp.arange(WIN_COLS, dtype=jnp.int32)
    lowest = WINDOW - here * tok_rows - block_index * TILE
    win_flags = (win_col[None, :] < WINDOW + TILE) & (win_col[None, :] >= lowest[:, None])
    sel_flags = jnp.repeat(listed, TILE, axis=1)
    colmask = jnp.concatenate([win_flags, sel_flags], axis=1).astype(jnp.int32)
    colmask = colmask.reshape(per_dev, 1, WIN_COLS + SEL_COLS)
    return block_attention(
        rows, ring_rows, from_ring, prev, queries, keys, values, colmask, tiles, ring, per_dev, scale
    )


def per_device(queries, keys, values, selection):
    tok_rows, head_size = keys.shape
    per_dev = tok_rows // TILE
    n_y = lax.axis_size("cy")
    n_z = lax.axis_size("cz")
    here = lax.axis_index("cy") * n_z + lax.axis_index("cz")

    both = jnp.stack(
        [keys.reshape(per_dev, TILE, head_size), values.reshape(per_dev, TILE, head_size)], axis=1
    )
    copies = jnp.broadcast_to(both[None], (n_y,) + both.shape)
    gathered = lax.all_to_all(copies, "cy", 0, 0, tiled=False)
    col_last = gathered[n_y - 1]
    gathered = lax.all_gather(gathered[: n_y - 1], "cz", axis=0, tiled=False)
    tiles = gathered.reshape(n_z * (n_y - 1) * per_dev, 2, TILE, head_size)
    ahead = [(i, (i + 1) % n_z) for i in range(n_z)]
    behind = [(i, (i - 1) % n_z) for i in range(n_z)]
    own = col_last
    by_distance = [own] + [None] * (n_z - 1)
    fwd = bwd = own
    for step in range(1, n_z // 2 + 1):
        fwd = lax.ppermute(fwd, "cz", ahead)
        by_distance[step] = fwd
        if step < n_z - step:
            bwd = lax.ppermute(bwd, "cz", behind)
            by_distance[n_z - step] = bwd
    ring = jnp.stack(by_distance).reshape(n_z * per_dev, 2, TILE, head_size)
    attended = device_attention(queries, keys, values, selection[0], tiles, ring, here, n_y, n_z)
    return lax.all_to_all(attended, "kvh", split_axis=0, concat_axis=1, tiled=True)


def solution(mesh):
    devices = mesh.devices
    ctx = devices.shape[0]
    z = len({tuple(d.coords)[2] for d in devices[:, 0]})
    z = z if ctx % z == 0 else ctx
    grid = Mesh(devices.reshape(ctx // z, z, devices.shape[1]), ("cy", "cz", "kvh"))
    row = P(("cy", "cz"), "kvh")
    return jax.shard_map(
        per_device,
        mesh=grid,
        in_specs=(row, row, row, P("kvh", ("cy", "cz"), None)),
        out_specs=P(("cy", "cz", "kvh"), None),
        check_vma=False,
    )
```

```python
import functools

import jax
import jax.numpy as jnp
from jax import lax
from jax.experimental import pallas as pl
from jax.experimental.pallas import tpu as pltpu
from jax.sharding import Mesh
from jax.sharding import PartitionSpec as P

TILE = 64
SEL = 16
WINDOW = 256
WIN_COLS = WINDOW + 2 * TILE
RING_ROWS = 2
SEL_COLS = SEL * TILE

masked_score = -1e30


def attention_kernel(
    rows_ref, ring_rows_ref, from_ring_ref, prev_ref, q_ref, keys_ref, values_ref, colmask_ref, tiles_hbm, ring_hbm,
    out_ref, selbuf, prevbuf, wink, winv, sems, prev_sem, *, per_dev, scale,
):
    head_size = keys_ref.shape[1]
    tok_rows = keys_ref.shape[0]
    heads = q_ref.shape[1] // head_size

    def fetch(b):
        slot = b % 2
        copies = []
        for i in range(SEL):
            k = b * SEL + i
            cp = pltpu.make_async_copy(tiles_hbm.at[rows_ref[k]], selbuf.at[slot, i], sems.at[slot, i])
            cr = pltpu.make_async_copy(ring_hbm.at[ring_rows_ref[k]], selbuf.at[slot, i], sems.at[slot, i])
            pl.when(from_ring_ref[k] == 0)(cp.start)
            pl.when(from_ring_ref[k] != 0)(cr.start)
            copies.append(cp)
        return copies

    prev_copy = pltpu.make_async_copy(tiles_hbm.at[pl.ds(prev_ref[0], per_dev)], prevbuf, prev_sem.at[0])
    prev_ring = pltpu.make_async_copy(ring_hbm.at[pl.ds(prev_ref[1], per_dev)], prevbuf, prev_sem.at[0])
    pl.when(prev_ref[2] == 0)(prev_copy.start)
    pl.when(prev_ref[2] != 0)(prev_ring.start)
    pending = fetch(0)
    wink[pl.ds(tok_rows, tok_rows), :] = keys_ref[...]
    winv[pl.ds(tok_rows, tok_rows), :] = values_ref[...]
    pad = wink.shape[0] - 2 * tok_rows
    wink[pl.ds(2 * tok_rows, pad), :] = jnp.zeros((pad, head_size), wink.dtype)
    winv[pl.ds(2 * tok_rows, pad), :] = jnp.zeros((pad, head_size), winv.dtype)
    prev_copy.wait()
    wink[pl.ds(0, tok_rows), :] = prevbuf[:, 0].reshape(tok_rows, head_size)
    winv[pl.ds(0, tok_rows), :] = prevbuf[:, 1].reshape(tok_rows, head_size)

    r = lax.broadcasted_iota(jnp.int32, (TILE, WIN_COLS), 0)
    j = lax.broadcasted_iota(jnp.int32, (TILE, WIN_COLS), 1)
    in_window = (j > r) & (j <= r + WINDOW)
    dims = (((1,), (1,)), ((), ()))
    for b in range(per_dev):
        for c in pending:
            c.wait()
        if b + 1 < per_dev:
            pending = fetch(b + 1)
        slot = b % 2
        q = q_ref[pl.ds(b * TILE, TILE), :]
        qs = jnp.concatenate([q[:, h * head_size : (h + 1) * head_size] for h in range(heads)], axis=0)
        k_win = wink[pl.ds(b * TILE, WIN_COLS), :]
        v_win = winv[pl.ds(b * TILE, WIN_COLS), :]
        k_sel = selbuf[slot, :, 0].reshape(SEL_COLS, head_size)
        v_sel = selbuf[slot, :, 1].reshape(SEL_COLS, head_size)
        mask = colmask_ref[b]
        win_ok = in_window & (mask[:, :WIN_COLS] > 0)
        sel_ok = mask[:, WIN_COLS:] > 0
        s_win = lax.dot_general(qs, k_win, dims, preferred_element_type=jnp.float32) * scale
        s_sel = lax.dot_general(qs, k_sel, dims, preferred_element_type=jnp.float32) * scale
        s_win = jnp.where(win_ok[None], s_win.reshape(heads, TILE, WIN_COLS), masked_score)
        s_win = s_win.reshape(heads * TILE, WIN_COLS)
        s_sel = jnp.where(sel_ok, s_sel, masked_score)
        peak = jnp.maximum(jnp.max(s_win, axis=1, keepdims=True), jnp.max(s_sel, axis=1, keepdims=True))
        w_win = jnp.exp(s_win - peak)
        w_sel = jnp.exp(s_sel - peak)
        total = jnp.sum(w_win, axis=1, keepdims=True) + jnp.sum(w_sel, axis=1, keepdims=True)
        num = jnp.dot(w_win.astype(jnp.bfloat16), v_win, preferred_element_type=jnp.float32)
        num = num + jnp.dot(w_sel.astype(jnp.bfloat16), v_sel, preferred_element_type=jnp.float32)
        res = (num / total).astype(out_ref.dtype)
        for h in range(heads):
            out_ref[pl.ds(b * TILE, TILE), h * head_size : (h + 1) * head_size] = res[h * TILE : (h + 1) * TILE]


def block_attention(rows, ring_rows, from_ring, prev, queries, keys, values, colmask, tiles, ring, per_dev, scale):
    tok_rows, width = queries.shape
    head_size = keys.shape[1]
    keys_per_block = WIN_COLS + SEL_COLS
    vmem = pltpu.MemorySpace.VMEM
    smem = pltpu.MemorySpace.SMEM
    return pl.pallas_call(
        functools.partial(attention_kernel, per_dev=per_dev, scale=scale),
        out_shape=jax.ShapeDtypeStruct((tok_rows, width), queries.dtype),
        in_specs=[
            pl.BlockSpec(memory_space=smem),
            pl.BlockSpec(memory_space=smem),
            pl.BlockSpec(memory_space=smem),
            pl.BlockSpec(memory_space=smem),
            pl.BlockSpec(memory_space=vmem),
            pl.BlockSpec(memory_space=vmem),
            pl.BlockSpec(memory_space=vmem),
            pl.BlockSpec(memory_space=vmem),
            pl.BlockSpec(memory_space=pl.ANY),
            pl.BlockSpec(memory_space=pl.ANY),
        ],
        out_specs=pl.BlockSpec(memory_space=vmem),
        scratch_shapes=[
            pltpu.VMEM((2, SEL, 2, TILE, head_size), tiles.dtype),
            pltpu.VMEM((per_dev, 2, TILE, head_size), tiles.dtype),
            pltpu.VMEM((2 * tok_rows + TILE, head_size), tiles.dtype),
            pltpu.VMEM((2 * tok_rows + TILE, head_size), tiles.dtype),
            pltpu.SemaphoreType.DMA((2, SEL)),
            pltpu.SemaphoreType.DMA((1,)),
        ],
        cost_estimate=pl.CostEstimate(
            flops=4 * tok_rows * width * keys_per_block,
            transcendentals=tok_rows * (width // head_size) * keys_per_block,
            bytes_accessed=2 * tok_rows * width * 2 + 2 * per_dev * SEL_COLS * head_size * 2,
        ),
    )(rows, ring_rows, from_ring, prev, queries, keys, values, colmask, tiles, ring)


def device_attention(queries, keys, values, lists, tiles, ring, here, n_y, n_z):
    tok_rows, head_size = keys.shape
    per_dev = tok_rows // TILE
    scale = 1.0 / head_size**0.5
    my_z = here % n_z

    def locate(tile_id):
        owner = tile_id // per_dev
        y, z = owner // n_z, owner % n_z
        in_ring = y >= n_y - RING_ROWS
        row = ((z * (n_y - RING_ROWS) + jnp.minimum(y, n_y - RING_ROWS - 1)) * per_dev + tile_id % per_dev)
        ring_row = (((my_z - z) % n_z) * RING_ROWS + jnp.maximum(y - (n_y - RING_ROWS), 0)) * per_dev
        row, ring_row = row.astype(jnp.int32), (ring_row + tile_id % per_dev).astype(jnp.int32)
        return row, ring_row, in_ring.astype(jnp.int32)

    listed = lists >= 0
    rows, ring_rows, from_ring = (a.reshape(-1) for a in locate(jnp.maximum(lists, 0)))
    prev_row, prev_ring_row, prev_in_ring = locate(jnp.maximum(here - 1, 0) * per_dev)
    prev = jnp.stack([prev_row, prev_ring_row, prev_in_ring]).astype(jnp.int32)

    block_index = jnp.arange(per_dev, dtype=jnp.int32)
    win_col = jnp.arange(WIN_COLS, dtype=jnp.int32)
    lowest = WINDOW - here * tok_rows - block_index * TILE
    win_flags = (win_col[None, :] < WINDOW + TILE) & (win_col[None, :] >= lowest[:, None])
    sel_flags = jnp.repeat(listed, TILE, axis=1)
    colmask = jnp.concatenate([win_flags, sel_flags], axis=1).astype(jnp.int32)
    colmask = colmask.reshape(per_dev, 1, WIN_COLS + SEL_COLS)
    return block_attention(
        rows, ring_rows, from_ring, prev, queries, keys, values, colmask, tiles, ring, per_dev, scale
    )


def per_device(queries, keys, values, selection):
    tok_rows, head_size = keys.shape
    per_dev = tok_rows // TILE
    n_y = lax.axis_size("cy")
    n_z = lax.axis_size("cz")
    here = lax.axis_index("cy") * n_z + lax.axis_index("cz")

    both = jnp.stack(
        [keys.reshape(per_dev, TILE, head_size), values.reshape(per_dev, TILE, head_size)], axis=1
    )
    copies = jnp.broadcast_to(both[None], (n_y,) + both.shape)
    gathered = lax.all_to_all(copies, "cy", 0, 0, tiled=False)
    col_last = gathered[n_y - RING_ROWS :]
    gathered_rest = lax.all_gather(gathered[: n_y - RING_ROWS], "cz", axis=0, tiled=False)
    tiles = gathered_rest.reshape(n_z * (n_y - RING_ROWS) * per_dev, 2, TILE, head_size)
    ahead = [(i, (i + 1) % n_z) for i in range(n_z)]
    behind = [(i, (i - 1) % n_z) for i in range(n_z)]
    own = col_last
    by_distance = [own] + [None] * (n_z - 1)
    fwd = bwd = own
    for step in range(1, n_z // 2 + 1):
        fwd = lax.ppermute(fwd, "cz", ahead)
        by_distance[step] = fwd
        if step < n_z - step:
            bwd = lax.ppermute(bwd, "cz", behind)
            by_distance[n_z - step] = bwd
    ring = jnp.stack(by_distance).reshape(n_z * RING_ROWS * per_dev, 2, TILE, head_size)
    attended = device_attention(queries, keys, values, selection[0], tiles, ring, here, n_y, n_z)
    return lax.all_to_all(attended, "kvh", split_axis=0, concat_axis=1, tiled=True)


def solution(mesh):
    devices = mesh.devices
    ctx = devices.shape[0]
    z = len({tuple(d.coords)[2] for d in devices[:, 0]})
    z = z if ctx % z == 0 else ctx
    grid = Mesh(devices.reshape(ctx // z, z, devices.shape[1]), ("cy", "cz", "kvh"))
    row = P(("cy", "cz"), "kvh")
    return jax.shard_map(
        per_device,
        mesh=grid,
        in_specs=(row, row, row, P("kvh", ("cy", "cz"), None)),
        out_specs=P(("cy", "cz", "kvh"), None),
        check_vma=False,
    )
```

```python
import functools

import jax
import jax.numpy as jnp
from jax import lax
from jax.experimental import pallas as pl
from jax.experimental.pallas import tpu as pltpu
from jax.sharding import Mesh
from jax.sharding import PartitionSpec as P

TILE = 64
SEL = 16
WINDOW = 256
WIN_COLS = WINDOW + 2 * TILE
SEL_COLS = SEL * TILE

masked_score = -1e30


def attention_kernel(
    rows_ref, ring_rows_ref, from_ring_ref, prev_ref, q_ref, keys_ref, values_ref, colmask_ref, tiles_hbm, ring_hbm,
    out_ref, selbuf, prevbuf, wink, winv, sems, prev_sem, *, per_dev, scale,
):
    head_size = keys_ref.shape[1]
    tok_rows = keys_ref.shape[0]
    heads = q_ref.shape[1] // head_size

    def fetch(b):
        slot = b % 2
        copies = []
        for i in range(SEL):
            k = b * SEL + i
            cp = pltpu.make_async_copy(tiles_hbm.at[rows_ref[k]], selbuf.at[slot, i], sems.at[slot, i])
            cr = pltpu.make_async_copy(ring_hbm.at[ring_rows_ref[k]], selbuf.at[slot, i], sems.at[slot, i])
            pl.when(from_ring_ref[k] == 0)(cp.start)
            pl.when(from_ring_ref[k] != 0)(cr.start)
            copies.append(cp)
        return copies

    prev_copy = pltpu.make_async_copy(tiles_hbm.at[pl.ds(prev_ref[0], per_dev)], prevbuf, prev_sem.at[0])
    prev_ring = pltpu.make_async_copy(ring_hbm.at[pl.ds(prev_ref[1], per_dev)], prevbuf, prev_sem.at[0])
    pl.when(prev_ref[2] == 0)(prev_copy.start)
    pl.when(prev_ref[2] != 0)(prev_ring.start)
    pending = fetch(0)
    wink[pl.ds(tok_rows, tok_rows), :] = keys_ref[...]
    winv[pl.ds(tok_rows, tok_rows), :] = values_ref[...]
    pad = wink.shape[0] - 2 * tok_rows
    wink[pl.ds(2 * tok_rows, pad), :] = jnp.zeros((pad, head_size), wink.dtype)
    winv[pl.ds(2 * tok_rows, pad), :] = jnp.zeros((pad, head_size), winv.dtype)
    prev_copy.wait()
    wink[pl.ds(0, tok_rows), :] = prevbuf[:, 0].reshape(tok_rows, head_size)
    winv[pl.ds(0, tok_rows), :] = prevbuf[:, 1].reshape(tok_rows, head_size)

    r = lax.broadcasted_iota(jnp.int32, (TILE, WIN_COLS), 0)
    j = lax.broadcasted_iota(jnp.int32, (TILE, WIN_COLS), 1)
    in_window = (j > r) & (j <= r + WINDOW)
    dims = (((1,), (1,)), ((), ()))
    for b in range(per_dev):
        for c in pending:
            c.wait()
        if b + 1 < per_dev:
            pending = fetch(b + 1)
        slot = b % 2
        q = q_ref[pl.ds(b * TILE, TILE), :]
        qs = jnp.concatenate([q[:, h * head_size : (h + 1) * head_size] for h in range(heads)], axis=0)
        k_win = wink[pl.ds(b * TILE, WIN_COLS), :]
        v_win = winv[pl.ds(b * TILE, WIN_COLS), :]
        k_sel = selbuf[slot, :, 0].reshape(SEL_COLS, head_size)
        v_sel = selbuf[slot, :, 1].reshape(SEL_COLS, head_size)
        mask = colmask_ref[b]
        win_ok = in_window & (mask[:, :WIN_COLS] > 0)
        sel_ok = mask[:, WIN_COLS:] > 0
        s_win = lax.dot_general(qs, k_win, dims, preferred_element_type=jnp.float32) * scale
        s_sel = lax.dot_general(qs, k_sel, dims, preferred_element_type=jnp.float32) * scale
        s_win = jnp.where(win_ok[None], s_win.reshape(heads, TILE, WIN_COLS), masked_score)
        s_win = s_win.reshape(heads * TILE, WIN_COLS)
        s_sel = jnp.where(sel_ok, s_sel, masked_score)
        peak = jnp.maximum(jnp.max(s_win, axis=1, keepdims=True), jnp.max(s_sel, axis=1, keepdims=True))
        w_win = jnp.exp(s_win - peak)
        w_sel = jnp.exp(s_sel - peak)
        total = jnp.sum(w_win, axis=1, keepdims=True) + jnp.sum(w_sel, axis=1, keepdims=True)
        num = jnp.dot(w_win.astype(jnp.bfloat16), v_win, preferred_element_type=jnp.float32)
        num = num + jnp.dot(w_sel.astype(jnp.bfloat16), v_sel, preferred_element_type=jnp.float32)
        res = (num / total).astype(out_ref.dtype)
        for h in range(heads):
            out_ref[pl.ds(b * TILE, TILE), h * head_size : (h + 1) * head_size] = res[h * TILE : (h + 1) * TILE]


def block_attention(rows, ring_rows, from_ring, prev, queries, keys, values, colmask, tiles, ring, per_dev, scale):
    tok_rows, width = queries.shape
    head_size = keys.shape[1]
    keys_per_block = WIN_COLS + SEL_COLS
    vmem = pltpu.MemorySpace.VMEM
    smem = pltpu.MemorySpace.SMEM
    return pl.pallas_call(
        functools.partial(attention_kernel, per_dev=per_dev, scale=scale),
        out_shape=jax.ShapeDtypeStruct((tok_rows, width), queries.dtype),
        in_specs=[
            pl.BlockSpec(memory_space=smem),
            pl.BlockSpec(memory_space=smem),
            pl.BlockSpec(memory_space=smem),
            pl.BlockSpec(memory_space=smem),
            pl.BlockSpec(memory_space=vmem),
            pl.BlockSpec(memory_space=vmem),
            pl.BlockSpec(memory_space=vmem),
            pl.BlockSpec(memory_space=vmem),
            pl.BlockSpec(memory_space=pl.ANY),
            pl.BlockSpec(memory_space=pl.ANY),
        ],
        out_specs=pl.BlockSpec(memory_space=vmem),
        scratch_shapes=[
            pltpu.VMEM((2, SEL, 2, TILE, head_size), tiles.dtype),
            pltpu.VMEM((per_dev, 2, TILE, head_size), tiles.dtype),
            pltpu.VMEM((2 * tok_rows + TILE, head_size), tiles.dtype),
            pltpu.VMEM((2 * tok_rows + TILE, head_size), tiles.dtype),
            pltpu.SemaphoreType.DMA((2, SEL)),
            pltpu.SemaphoreType.DMA((1,)),
        ],
        cost_estimate=pl.CostEstimate(
            flops=4 * tok_rows * width * keys_per_block,
            transcendentals=tok_rows * (width // head_size) * keys_per_block,
            bytes_accessed=2 * tok_rows * width * 2 + 2 * per_dev * SEL_COLS * head_size * 2,
        ),
    )(rows, ring_rows, from_ring, prev, queries, keys, values, colmask, tiles, ring)


def device_attention(queries, keys, values, lists, tiles, ring, here, n_y, n_z):
    tok_rows, head_size = keys.shape
    per_dev = tok_rows // TILE
    scale = 1.0 / head_size**0.5
    my_z = here % n_z
    my_y = here // n_z

    def locate(tile_id):
        owner = tile_id // per_dev
        y, z = owner // n_z, owner % n_z
        in_ring = y == my_y
        slot = jnp.clip(y - (y > my_y).astype(y.dtype), 0, n_y - 2)
        row = ((z * (n_y - 1) + slot) * per_dev + tile_id % per_dev).astype(jnp.int32)
        ring_row = (((my_z - z) % n_z) * per_dev + tile_id % per_dev).astype(jnp.int32)
        return row, ring_row, in_ring.astype(jnp.int32)

    listed = lists >= 0
    rows, ring_rows, from_ring = (a.reshape(-1) for a in locate(jnp.maximum(lists, 0)))
    prev_row, prev_ring_row, prev_in_ring = locate(jnp.maximum(here - 1, 0) * per_dev)
    prev = jnp.stack([prev_row, prev_ring_row, prev_in_ring]).astype(jnp.int32)

    block_index = jnp.arange(per_dev, dtype=jnp.int32)
    win_col = jnp.arange(WIN_COLS, dtype=jnp.int32)
    lowest = WINDOW - here * tok_rows - block_index * TILE
    win_flags = (win_col[None, :] < WINDOW + TILE) & (win_col[None, :] >= lowest[:, None])
    sel_flags = jnp.repeat(listed, TILE, axis=1)
    colmask = jnp.concatenate([win_flags, sel_flags], axis=1).astype(jnp.int32)
    colmask = colmask.reshape(per_dev, 1, WIN_COLS + SEL_COLS)
    return block_attention(
        rows, ring_rows, from_ring, prev, queries, keys, values, colmask, tiles, ring, per_dev, scale
    )


def per_device(queries, keys, values, selection):
    tok_rows, head_size = keys.shape
    per_dev = tok_rows // TILE
    n_y = lax.axis_size("cy")
    n_z = lax.axis_size("cz")
    here = lax.axis_index("cy") * n_z + lax.axis_index("cz")

    both = jnp.stack(
        [keys.reshape(per_dev, TILE, head_size), values.reshape(per_dev, TILE, head_size)], axis=1
    )
    copies = jnp.broadcast_to(both[None], (n_y,) + both.shape)
    gathered = lax.all_to_all(copies, "cy", 0, 0, tiled=False)
    col_last = both
    my_y = lax.axis_index("cy")
    others = jnp.arange(n_y - 1, dtype=jnp.int32)
    others = others + (others >= my_y).astype(jnp.int32)
    gathered = lax.all_gather(jnp.take(gathered, others, axis=0), "cz", axis=0, tiled=False)
    tiles = gathered.reshape(n_z * (n_y - 1) * per_dev, 2, TILE, head_size)
    ahead = [(i, (i + 1) % n_z) for i in range(n_z)]
    behind = [(i, (i - 1) % n_z) for i in range(n_z)]
    own = col_last
    by_distance = [own] + [None] * (n_z - 1)
    fwd = bwd = own
    for step in range(1, n_z // 2 + 1):
        fwd = lax.ppermute(fwd, "cz", ahead)
        by_distance[step] = fwd
        if step < n_z - step:
            bwd = lax.ppermute(bwd, "cz", behind)
            by_distance[n_z - step] = bwd
    ring = jnp.stack(by_distance).reshape(n_z * per_dev, 2, TILE, head_size)
    attended = device_attention(queries, keys, values, selection[0], tiles, ring, here, n_y, n_z)
    return lax.all_to_all(attended, "kvh", split_axis=0, concat_axis=1, tiled=True)


def solution(mesh):
    devices = mesh.devices
    ctx = devices.shape[0]
    z = len({tuple(d.coords)[2] for d in devices[:, 0]})
    z = z if ctx % z == 0 else ctx
    grid = Mesh(devices.reshape(ctx // z, z, devices.shape[1]), ("cy", "cz", "kvh"))
    row = P(("cy", "cz"), "kvh")
    return jax.shard_map(
        per_device,
        mesh=grid,
        in_specs=(row, row, row, P("kvh", ("cy", "cz"), None)),
        out_specs=P(("cy", "cz", "kvh"), None),
        check_vma=False,
    )
```
